256 devices in a mesh: row: 4 (over z_lo), col: 16 (over z_hi, y, core), layer: 4 (over x).
Axes of the slice: x: 4, y: 4, z: 8 (z_hi: 2, z_lo: 4; z = z_hi * 4 + z_lo), core: 2. Of those that a mesh axis runs over, the one named last changes fastest.
Arguments:
- left_blocks: bfloat16 [4096, 131072], P('row', ('layer', 'col')), may hold values from -6 to 6
- left_pattern: int32 [64, 2048], P('row', ('layer', 'col')), may hold values 0 or 1
- right_blocks: bfloat16 [131072, 2048], P(('layer', 'col'), 'row'), may hold values from -0.09375 to 0.09375
- right_pattern: int32 [2048, 32], P(('layer', 'col'), 'row'), may hold values 0 or 1
Outputs:
- product: bfloat16 [4096, 2048], P('row', ('col', 'layer'))
The draws below stay inside these ranges and needn't reach their ends.
All inputs are finite; a program needn't handle non-finite values. No bound on the sum of `left_pattern` or of `right_pattern` on one device may be relied on, other than what follows from the above.
Results may differ from the reference program's by a relative error of at most 0.001.
Values may be sent and summed in bfloat16 or wider, within the bound.
No kernel may reach another device: no remote copies, remote signals or barrier semaphores. Data moves between devices by JAX's collectives and lax.ppermute only.
A program may use at most 64 MiB of HBM per device.

```python
import jax
import jax.numpy as jnp

BS = 64
M = 4096
K = 131072
N = 2048


def set_ends(array, own_key, low, largest):
    place = [jax.random.randint(jax.random.fold_in(own_key, axis), (), 0, length) for axis, length in enumerate(array.shape)]
    widest = array.shape.index(max(array.shape))
    neighbour = place[:widest] + [(place[widest] + 1) % array.shape[widest]] + place[widest + 1:]
    return array.at[tuple(place)].set(low).at[tuple(neighbour)].set(largest)


def with_spikes(drawn, key, source, target, blocks, factor):
    owner, partner = [(jnp.arange(drawn.shape[position]) // (drawn.shape[position] // blocks)).reshape([-1 if axis == position else 1 for axis in range(drawn.ndim)]) for position in (source, target)]
    chosen = jax.random.permutation(key, blocks)[partner]
    strong = (owner == chosen) | (owner == (partner + blocks // 2) % blocks)
    return jnp.where(strong, factor * drawn, drawn)


def block_levels(stream_key, extent, pieces, least, top_value):
    factor_of = 1.0
    for position, blocks in pieces:
        heights = jax.random.uniform(jax.random.fold_in(jax.random.fold_in(stream_key, 6), position), (blocks,), jnp.float32, least / len(pieces), top_value / len(pieces))
        factor_of = factor_of * jnp.repeat(jnp.exp(heights), extent[position] // blocks).reshape((-1,) + (1,) * (len(extent) - 1 - position))
    return factor_of


def gaussian(stream_key, shape, deviation, most, shards=(), held_as=jnp.bfloat16):
    level = block_levels(stream_key, shape, shards, -0.22, 0.18) if shards else 1.0
    entries = jax.random.normal(stream_key, shape, jnp.float32) * deviation * level
    return jnp.minimum(jnp.maximum(entries, -most), most).astype(held_as)


def bell_draw_with(own_key, dims, width, limit, split, heavy, dtype=jnp.bfloat16):
    values = width * jax.random.normal(own_key, dims, jnp.float32)
    if split:
        values = values * block_levels(own_key, dims, split, -0.22, 0.18)
    return jnp.clip(with_spikes(values, jax.random.fold_in(own_key, 3), *heavy), -limit, limit).astype(dtype)


def setup_inputs(seed: int = 0) -> dict:
    keys = jax.random.split(jax.random.key(seed), 5)
    return {
        "left_blocks": gaussian(keys[0], (M, K), 1.0, 6.0, ((0, 4), (1, 64))),
        "left_pattern": set_ends((jax.random.randint(keys[1], (M // BS, K // BS), 0, 2) < 1).astype(jnp.int32), jax.random.fold_in(keys[1], 1), 0, 1),
        "right_blocks": bell_draw_with(keys[2], (K, N), (K // 4) ** -0.5, 0.09375, ((0, 64), (1, 4)), (0, 1, 64, 4.0)),
        "right_pattern": set_ends((jax.random.randint(keys[3], (K // BS, N // BS), 0, 2) < 1).astype(jnp.int32), jax.random.fold_in(keys[3], 1), 0, 1),
    }


def apply_pattern(values, pattern):
    rows, cols = values.shape
    shaped = values.reshape(rows // BS, BS, cols // BS, BS)
    masked = shaped * pattern[:, None, :, None].astype(jnp.bfloat16)
    return masked.reshape(rows, cols)


def reference(left_blocks, left_pattern, right_blocks, right_pattern):
    left = apply_pattern(left_blocks, left_pattern)
    right = apply_pattern(right_blocks, right_pattern)
    return jnp.dot(left, right, preferred_element_type=jnp.float32).astype(jnp.bfloat16)
```

```python
import jax
import jax.numpy as jnp
from jax import lax
from jax.sharding import Mesh
from jax.sharding import PartitionSpec as P

COL_PARTS = ("zhi", "y", "core")


def from_behind(x, axis, by):
    size = lax.axis_size(axis)
    return lax.ppermute(x, axis, [(i, (i + by) % size) for i in range(size)])


def apply_pattern(values, pattern):
    rows, cols = values.shape
    block = rows // pattern.shape[0]
    shaped = values.reshape(pattern.shape[0], block, pattern.shape[1], block)
    masked = shaped * pattern[:, None, :, None].astype(jnp.bfloat16)
    return masked.reshape(rows, cols)


def local(left_blocks, left_pattern, right_blocks, right_pattern):
    left = apply_pattern(left_blocks, left_pattern)
    right = apply_pattern(right_blocks, right_pattern)
    left_rows = left.shape[0]
    range_cols = right.shape[1]
    cycle_size = lax.axis_size("row")
    position = lax.axis_index("row")
    partial_t = jnp.zeros((range_cols * cycle_size, left_rows), jnp.float32)
    current = right
    for step in range(cycle_size):
        if step > 0:
            current = from_behind(current, "row", 1)
        owner = (position - step) % cycle_size
        piece = lax.dot_general(current, left, (((0,), (1,)), ((), ())), preferred_element_type=jnp.float32)
        partial_t = lax.dynamic_update_slice_in_dim(partial_t, piece, owner * range_cols, 0)
    zhi, ys, cores, layers = (lax.axis_size(a) for a in COL_PARTS + ("layer",))
    block = partial_t.shape[0] // (zhi * ys * cores * layers)
    ordered = partial_t.reshape(zhi, ys, cores, layers, block, left_rows)
    ordered = ordered.transpose(2, 3, 1, 0, 4, 5).reshape(-1, left_rows)
    for axis in ("core", "layer", "y", "zhi"):
        ordered = lax.psum_scatter(ordered, axis, scatter_dimension=0, tiled=True)
    return ordered.T.astype(jnp.bfloat16)


def solution(mesh):
    cols = mesh.shape["col"]
    fine = Mesh(
        mesh.devices.reshape(mesh.shape["row"], 2, cols // 4, 2, mesh.shape["layer"]),
        ("row",) + COL_PARTS + ("layer",),
    )
    inner = ("layer",) + COL_PARTS
    placed = (
        P("row", inner),
        P("row", inner),
        P(inner, "row"),
        P(inner, "row"),
    )
    return jax.shard_map(
        local, mesh=fine, in_specs=placed, out_specs=P("row", COL_PARTS + ("layer",)), check_vma=False
    )
```

```python
import jax
import jax.numpy as jnp
from jax import lax
from jax.sharding import Mesh
from jax.sharding import PartitionSpec as P

COL_PARTS = ("zhi", "y", "core")


def from_behind(x, axis, by):
    size = lax.axis_size(axis)
    return lax.ppermute(x, axis, [(i, (i + by) % size) for i in range(size)])


def apply_pattern(values, pattern):
    rows, cols = values.shape
    block = rows // pattern.shape[0]
    widened = jnp.repeat(pattern.astype(jnp.bfloat16), cols // pattern.shape[1], axis=1)
    masked = values.reshape(pattern.shape[0], block, cols) * widened[:, None, :]
    return masked.reshape(rows, cols)


def halve_over(x, axis):
    half = x.shape[0] // 2
    first = lax.axis_index(axis) == 0
    keep = jnp.where(first, x[:half], x[half:])
    send = jnp.where(first, x[half:], x[:half])
    return keep + lax.ppermute(send, axis, [(0, 1), (1, 0)])


def spread_over(x, axis):
    n = lax.axis_size(axis)
    x = x.reshape(n, x.shape[0] // n, *x.shape[1:])
    return lax.all_to_all(x, axis, 0, 0, tiled=False).sum(0)


def local(left_blocks, left_pattern, right_blocks, right_pattern):
    left = apply_pattern(left_blocks, left_pattern)
    right = apply_pattern(right_blocks, right_pattern)
    left_rows = left.shape[0]
    cycle_size = lax.axis_size("row")
    position = lax.axis_index("row")
    zhi, ys, cores, layers = (lax.axis_size(a) for a in COL_PARTS + ("layer",))
    halves = ys // 2
    block = right.shape[1] // (halves * cores * layers)
    gathered = jnp.zeros((cycle_size, halves, block, left_rows), jnp.float32)
    current = right
    for step in range(cycle_size):
        if step > 0:
            current = from_behind(current, "row", 1)
        owner = (position - step) % cycle_size
        piece = lax.dot_general(current, left, (((0,), (1,)), ((), ())), preferred_element_type=jnp.float32)
        piece = piece.reshape(halves, cores, layers, block, left_rows).transpose(1, 2, 0, 3, 4)
        piece = halve_over(piece.reshape(cores * layers, halves, block, left_rows), "core")
        piece = spread_over(piece, "layer")
        gathered = lax.dynamic_update_slice_in_dim(gathered, piece, owner, 0)
    ordered = gathered.reshape(zhi, ys, block, left_rows).transpose(1, 0, 2, 3)
    ordered = spread_over(ordered, "y")[0]
    ordered = halve_over(ordered, "zhi")
    return ordered.reshape(block, left_rows).T.astype(jnp.bfloat16)


def solution(mesh):
    cols = mesh.shape["col"]
    fine = Mesh(
        mesh.devices.reshape(mesh.shape["row"], 2, cols // 4, 2, mesh.shape["layer"]),
        ("row",) + COL_PARTS + ("layer",),
    )
    inner = ("layer",) + COL_PARTS
    placed = (
        P("row", inner),
        P("row", inner),
        P(inner, "row"),
        P(inner, "row"),
    )
    return jax.shard_map(
        local, mesh=fine, in_specs=placed, out_specs=P("row", COL_PARTS + ("layer",)), check_vma=False
    )
```

```python
import jax
import jax.numpy as jnp
from jax import lax
from jax.sharding import Mesh
from jax.sharding import PartitionSpec as P

COL_PARTS = ("zhi", "y", "core")


def from_behind(x, axis, by):
    size = lax.axis_size(axis)
    return lax.ppermute(x, axis, [(i, (i + by) % size) for i in range(size)])


def apply_pattern(values, pattern):
    rows, cols = values.shape
    block = rows // pattern.shape[0]
    widened = jnp.repeat(pattern.astype(jnp.bfloat16), cols // pattern.shape[1], axis=1)
    masked = values.reshape(pattern.shape[0], block, cols) * widened[:, None, :]
    return masked.reshape(rows, cols)


def halve_over(x, axis):
    half = x.shape[0] // 2
    index = lax.axis_index(axis)
    keep = lax.dynamic_slice_in_dim(x, index * half, half, 0)
    send = lax.dynamic_slice_in_dim(x, (1 - index) * half, half, 0)
    return keep + lax.ppermute(send, axis, [(0, 1), (1, 0)])


def spread_over(x, axis):
    n = lax.axis_size(axis)
    x = x.reshape(n, x.shape[0] // n, *x.shape[1:])
    return lax.all_to_all(x, axis, 0, 0, tiled=False).sum(0)


def local(left_blocks, left_pattern, right_blocks, right_pattern):
    left = apply_pattern(left_blocks, left_pattern)
    right = apply_pattern(right_blocks, right_pattern)
    left_rows = left.shape[0]
    cycle_size = lax.axis_size("row")
    position = lax.axis_index("row")
    zhi, ys, cores, layers = (lax.axis_size(a) for a in COL_PARTS + ("layer",))
    halves = ys // 2
    block = right.shape[1] // (halves * cores * layers)
    right = right.reshape(-1, halves, cores, layers, block).transpose(0, 2, 3, 1, 4).reshape(right.shape)
    gathered = jnp.zeros((cycle_size, halves, block, left_rows), jnp.float32)
    current = right
    reduced = None
    for step in range(cycle_size):
        if step > 0:
            current = from_behind(current, "row", 1)
            current, reduced = lax.optimization_barrier((current, reduced))
            gathered = lax.dynamic_update_slice_in_dim(gathered, reduced, (position - step + 1) % cycle_size, 0)
        piece = lax.dot_general(current, left, (((0,), (1,)), ((), ())), preferred_element_type=jnp.float32)
        piece = halve_over(piece.reshape(cores * layers, halves, block, left_rows), "core")
        reduced = spread_over(piece, "layer")
    gathered = lax.dynamic_update_slice_in_dim(gathered, reduced, (position + 1) % cycle_size, 0)
    ordered = gathered.reshape(zhi, ys, block, left_rows).transpose(1, 0, 2, 3)
    ordered = spread_over(ordered, "y")[0]
    ordered = halve_over(ordered, "zhi")
    return ordered.reshape(block, left_rows).T.astype(jnp.bfloat16)


def solution(mesh):
    cols = mesh.shape["col"]
    fine = Mesh(
        mesh.devices.reshape(mesh.shape["row"], 2, cols // 4, 2, mesh.shape["layer"]),
        ("row",) + COL_PARTS + ("layer",),
    )
    inner = ("layer",) + COL_PARTS
    placed = (
        P("row", inner),
        P("row", inner),
        P(inner, "row"),
        P(inner, "row"),
    )
    return jax.shard_map(
        local, mesh=fine, in_specs=placed, out_specs=P("row", COL_PARTS + ("layer",)), check_vma=False
    )
```

```python
import jax
import jax.numpy as jnp
from jax import lax
from jax.sharding import Mesh
from jax.sharding import PartitionSpec as P

COL_PARTS = ("zhi", "y", "core")


def from_behind(x, axis, by):
    size = lax.axis_size(axis)
    return lax.ppermute(x, axis, [(i, (i + by) % size) for i in range(size)])


def apply_pattern(values, pattern):
    rows, cols = values.shape
    block = rows // pattern.shape[0]
    widened = jnp.repeat(pattern.astype(jnp.bfloat16), cols // pattern.shape[1], axis=1)
    masked = values.reshape(pattern.shape[0], block, cols) * widened[:, None, :]
    return masked.reshape(rows, cols)


def halve_over(x, axis):
    half = x.shape[0] // 2
    index = lax.axis_index(axis)
    keep = lax.dynamic_slice_in_dim(x, index * half, half, 0)
    send = lax.dynamic_slice_in_dim(x, (1 - index) * half, half, 0)
    return keep + lax.ppermute(send, axis, [(0, 1), (1, 0)])


def spread_over(x, axis):
    n = lax.axis_size(axis)
    index = lax.axis_index(axis)
    total = lax.dynamic_index_in_dim(x, index, 0, keepdims=False)
    for shift in range(1, n):
        send = lax.dynamic_index_in_dim(x, (index + shift) % n, 0, keepdims=False)
        total = total + lax.ppermute(send, axis, [(i, (i + shift) % n) for i in range(n)])
    return total


def local(left_blocks, left_pattern, right_blocks, right_pattern):
    left = apply_pattern(left_blocks, left_pattern)
    right = apply_pattern(right_blocks, right_pattern)
    left_rows = left.shape[0]
    cycle_size = lax.axis_size("row")
    position = lax.axis_index("row")
    zhi, ys, cores, layers = (lax.axis_size(a) for a in COL_PARTS + ("layer",))
    halves = ys // 2
    block = right.shape[1] // (halves * cores * layers)
    gathered = jnp.zeros((cycle_size, halves, block, left_rows), jnp.float32)
    arrived = right
    reduced = None
    for step in range(cycle_size):
        current = arrived
        if step > 0:
            current, reduced = lax.optimization_barrier((current, reduced))
            gathered = lax.dynamic_update_slice_in_dim(gathered, reduced[None], (position - step + 1) % cycle_size, 0)
        if step + 1 < cycle_size:
            arrived = from_behind(arrived, "row", 1)
        current = current.reshape(-1, halves, cores, layers, block).transpose(0, 2, 3, 1, 4)
        piece = lax.dot_general(current, left, (((0,), (1,)), ((), ())), preferred_element_type=jnp.float32)
        piece = halve_over(piece.reshape(cores * layers, halves, block, left_rows), "core")
        reduced = spread_over(piece, "layer")
    gathered = lax.dynamic_update_slice_in_dim(gathered, reduced[None], (position + 1) % cycle_size, 0)
    ordered = gathered.reshape(zhi, ys, block, left_rows).transpose(1, 0, 2, 3)
    ordered = spread_over(ordered, "y")
    ordered = halve_over(ordered, "zhi")
    return ordered.reshape(block, left_rows).T.astype(jnp.bfloat16)


def solution(mesh):
    cols = mesh.shape["col"]
    fine = Mesh(
        mesh.devices.reshape(mesh.shape["row"], 2, cols // 4, 2, mesh.shape["layer"]),
        ("row",) + COL_PARTS + ("layer",),
    )
    inner = ("layer",) + COL_PARTS
    placed = (
        P("row", inner),
        P("row", inner),
        P(inner, "row"),
        P(inner, "row"),
    )
    return jax.shard_map(
        local, mesh=fine, in_specs=placed, out_specs=P("row", COL_PARTS + ("layer",)), check_vma=False
    )
```

```python
import jax
import jax.numpy as jnp
from jax import lax
from jax.sharding import Mesh
from jax.sharding import PartitionSpec as P

COL_PARTS = ("zhi", "y", "core")


def from_behind(x, axis, by):
    size = lax.axis_size(axis)
    return lax.ppermute(x, axis, [(i, (i + by) % size) for i in range(size)])


def apply_pattern(values, pattern):
    rows, cols = values.shape
    block = rows // pattern.shape[0]
    widened = jnp.repeat(pattern.astype(jnp.bfloat16), cols // pattern.shape[1], axis=1)
    masked = values.reshape(pattern.shape[0], block, cols) * widened[:, None, :]
    return masked.reshape(rows, cols)


def pair_over(x, axis, dim):
    index = lax.axis_index(axis)
    keep = lax.dynamic_index_in_dim(x, index, dim, keepdims=False)
    send = lax.dynamic_index_in_dim(x, 1 - index, dim, keepdims=False)
    return keep + lax.ppermute(send, axis, [(0, 1), (1, 0)])


def spread_over(x, axis, dim):
    n = lax.axis_size(axis)
    index = lax.axis_index(axis)
    total = lax.dynamic_index_in_dim(x, index, dim, keepdims=False)
    for shift in range(1, n):
        send = lax.dynamic_index_in_dim(x, (index + shift) % n, dim, keepdims=False)
        total = total + lax.ppermute(send, axis, [(i, (i + shift) % n) for i in range(n)])
    return total


def local(left_blocks, left_pattern, right_blocks, right_pattern):
    left = apply_pattern(left_blocks, left_pattern)
    right = apply_pattern(right_blocks, right_pattern)
    left_rows = left.shape[0]
    cycle_size = lax.axis_size("row")
    position = lax.axis_index("row")
    zhi, ys, cores, layers = (lax.axis_size(a) for a in COL_PARTS + ("layer",))
    halves = ys // 2
    block = right.shape[1] // (halves * cores * layers)
    mine = lax.axis_index("zhi") * 2 + lax.axis_index("y") // halves
    result = jnp.zeros((block, left_rows), jnp.float32)
    arrived = right
    reduced = None
    for step in range(cycle_size):
        current = arrived
        if step > 0:
            current, reduced = lax.optimization_barrier((current, reduced))
            result = jnp.where(mine == (position - step + 1) % cycle_size, reduced, result)
        if step + 1 < cycle_size:
            arrived = from_behind(arrived, "row", 1)
        owner = (position - step) % cycle_size
        piece = lax.dot_general(current, left, (((0,), (1,)), ((), ())), preferred_element_type=jnp.float32)
        piece = piece.reshape(halves, cores, layers, block, left_rows)
        piece = pair_over(piece, "core", 1)
        piece = spread_over(piece, "layer", 1)
        spread = lax.dynamic_update_slice_in_dim(
            jnp.zeros((ys, block, left_rows), jnp.float32), piece, (owner % 2) * halves, 0
        )
        piece = spread_over(spread, "y", 0)
        reduced = piece + lax.ppermute(piece, "zhi", [(0, 1), (1, 0)])
    result = jnp.where(mine == (position + 1) % cycle_size, reduced, result)
    return result.T.astype(jnp.bfloat16)


def solution(mesh):
    cols = mesh.shape["col"]
    fine = Mesh(
        mesh.devices.reshape(mesh.shape["row"], 2, cols // 4, 2, mesh.shape["layer"]),
        ("row",) + COL_PARTS + ("layer",),
    )
    inner = ("layer",) + COL_PARTS
    placed = (
        P("row", inner),
        P("row", inner),
        P(inner, "row"),
        P(inner, "row"),
    )
    return jax.shard_map(
        local, mesh=fine, in_specs=placed, out_specs=P("row", COL_PARTS + ("layer",)), check_vma=False
    )
```

```python
import jax
import jax.numpy as jnp
from jax import lax
from jax.sharding import Mesh
from jax.sharding import PartitionSpec as P

COL_PARTS = ("zhi", "y", "core")


def from_behind(x, axis, by):
    size = lax.axis_size(axis)
    return lax.ppermute(x, axis, [(i, (i + by) % size) for i in range(size)])


def apply_pattern(values, pattern):
    rows, cols = values.shape
    block = rows // pattern.shape[0]
    widened = jnp.repeat(pattern.astype(jnp.bfloat16), cols // pattern.shape[1], axis=1)
    masked = values.reshape(pattern.shape[0], block, cols) * widened[:, None, :]
    return masked.reshape(rows, cols)


def pair_over(x, axis, dim):
    index = lax.axis_index(axis)
    keep = lax.dynamic_index_in_dim(x, index, dim, keepdims=False)
    send = lax.dynamic_index_in_dim(x, 1 - index, dim, keepdims=False)
    return keep + lax.ppermute(send, axis, [(0, 1), (1, 0)])


def spread_over(x, axes, dim):
    n = x.shape[dim]
    index = lax.axis_index(axes)
    total = lax.dynamic_index_in_dim(x, index, dim, keepdims=False)
    for shift in range(1, n):
        send = lax.dynamic_index_in_dim(x, (index + shift) % n, dim, keepdims=False)
        total = total + lax.ppermute(send, axes, [(i, (i + shift) % n) for i in range(n)])
    return total


def local(left_blocks, left_pattern, right_blocks, right_pattern):
    left = apply_pattern(left_blocks, left_pattern)
    right = apply_pattern(right_blocks, right_pattern)
    left_rows = left.shape[0]
    cycle_size = lax.axis_size("row")
    position = lax.axis_index("row")
    zhi, ys, cores, layers = (lax.axis_size(a) for a in COL_PARTS + ("layer",))
    halves = ys // 2
    block = right.shape[1] // (halves * cores * layers)
    gathered = jnp.zeros((cycle_size, halves, block, left_rows), jnp.float32)
    arrived = right
    reduced = None
    for step in range(cycle_size):
        current = arrived
        if step > 0:
            current, reduced = lax.optimization_barrier((current, reduced))
            gathered = lax.dynamic_update_slice_in_dim(gathered, reduced[None], (position - step + 1) % cycle_size, 0)
        if step + 1 < cycle_size:
            arrived = from_behind(arrived, "row", 1)
        piece = lax.dot_general(current, left, (((0,), (1,)), ((), ())), preferred_element_type=jnp.float32)
        piece = piece.reshape(halves, cores, layers, block, left_rows)
        piece = pair_over(piece, "core", 1)
        reduced = spread_over(piece, "layer", 1)
    gathered = lax.dynamic_update_slice_in_dim(gathered, reduced[None], (position + 1) % cycle_size, 0)
    ordered = spread_over(gathered.reshape(zhi * ys, block, left_rows), ("zhi", "y"), 0)
    return ordered.T.astype(jnp.bfloat16)


def solution(mesh):
    cols = mesh.shape["col"]
    fine = Mesh(
        mesh.devices.reshape(mesh.shape["row"], 2, cols // 4, 2, mesh.shape["layer"]),
        ("row",) + COL_PARTS + ("layer",),
    )
    inner = ("layer",) + COL_PARTS
    placed = (
        P("row", inner),
        P("row", inner),
        P(inner, "row"),
        P(inner, "row"),
    )
    return jax.shard_map(
        local, mesh=fine, in_specs=placed, out_specs=P("row", COL_PARTS + ("layer",)), check_vma=False
    )
```

```python
import jax
import jax.numpy as jnp
from jax import lax
from jax.sharding import Mesh
from jax.sharding import PartitionSpec as P

COL_PARTS = ("zhi", "y", "core")


def from_behind(x, axis, by):
    size = lax.axis_size(axis)
    return lax.ppermute(x, axis, [(i, (i + by) % size) for i in range(size)])


def apply_pattern(values, pattern):
    rows, cols = values.shape
    block = rows // pattern.shape[0]
    widened = jnp.repeat(pattern.astype(jnp.bfloat16), cols // pattern.shape[1], axis=1)
    masked = values.reshape(pattern.shape[0], block, cols) * widened[:, None, :]
    return masked.reshape(rows, cols)


def pair_over(x, axis, dim):
    index = lax.axis_index(axis)
    keep = lax.dynamic_index_in_dim(x, index, dim, keepdims=False)
    send = lax.dynamic_index_in_dim(x, 1 - index, dim, keepdims=False)
    return keep + lax.ppermute(send, axis, [(0, 1), (1, 0)])


def spread_over(x, axes, dim):
    n = x.shape[dim]
    index = lax.axis_index(axes)
    total = lax.dynamic_index_in_dim(x, index, dim, keepdims=False)
    for shift in range(1, n):
        send = lax.dynamic_index_in_dim(x, (index + shift) % n, dim, keepdims=False)
        total = total + lax.ppermute(send, axes, [(i, (i + shift) % n) for i in range(n)])
    return total


def local(left_blocks, left_pattern, right_blocks, right_pattern):
    left = apply_pattern(left_blocks, left_pattern)
    right = apply_pattern(right_blocks, right_pattern).T
    left_rows = left.shape[0]
    cycle_size = lax.axis_size("row")
    position = lax.axis_index("row")
    zhi, ys, cores, layers = (lax.axis_size(a) for a in COL_PARTS + ("layer",))
    halves = ys // 2
    block = right.shape[0] // (halves * cores * layers)
    gathered = jnp.zeros((cycle_size, halves, block, left_rows), jnp.float32)
    arrived = right
    reduced = None
    for step in range(cycle_size):
        current = arrived
        if step > 0:
            current, reduced = lax.optimization_barrier((current, reduced))
            gathered = lax.dynamic_update_slice_in_dim(gathered, reduced[None], (position - step + 1) % cycle_size, 0)
        if step + 1 < cycle_size:
            arrived = from_behind(current, "row", 1)
        piece = lax.dot_general(current, left, (((1,), (1,)), ((), ())), preferred_element_type=jnp.float32)
        piece = piece.reshape(halves, cores, layers, block, left_rows)
        piece = pair_over(piece, "core", 1)
        reduced = spread_over(piece, "layer", 1)
    gathered = lax.dynamic_update_slice_in_dim(gathered, reduced[None], (position + 1) % cycle_size, 0)
    ordered = gathered.reshape(zhi, ys, block, left_rows)
    ordered = spread_over(ordered, "y", 1)
    ordered = pair_over(ordered, "zhi", 0)
    return ordered.T.astype(jnp.bfloat16)


def solution(mesh):
    cols = mesh.shape["col"]
    fine = Mesh(
        mesh.devices.reshape(mesh.shape["row"], 2, cols // 4, 2, mesh.shape["layer"]),
        ("row",) + COL_PARTS + ("layer",),
    )
    inner = ("layer",) + COL_PARTS
    placed = (
        P("row", inner),
        P("row", inner),
        P(inner, "row"),
        P(inner, "row"),
    )
    return jax.shard_map(
        local, mesh=fine, in_specs=placed, out_specs=P("row", COL_PARTS + ("layer",)), check_vma=False
    )
```

```python
import jax
import jax.numpy as jnp
from jax import lax
from jax.sharding import Mesh
from jax.sharding import PartitionSpec as P

COL_PARTS = ("zhi", "y", "core")


def from_behind(x, axis, by):
    size = lax.axis_size(axis)
    return lax.ppermute(x, axis, [(i, (i + by) % size) for i in range(size)])


def apply_pattern(values, pattern):
    rows, cols = values.shape
    block = rows // pattern.shape[0]
    widened = jnp.repeat(pattern.astype(jnp.bfloat16), cols // pattern.shape[1], axis=1)
    masked = values.reshape(pattern.shape[0], block, cols) * widened[:, None, :]
    return masked.reshape(rows, cols)


def pair_over(x, axis, dim):
    index = lax.axis_index(axis)
    keep = lax.dynamic_index_in_dim(x, index, dim, keepdims=False)
    send = lax.dynamic_index_in_dim(x, 1 - index, dim, keepdims=False)
    return keep + lax.ppermute(send, axis, [(0, 1), (1, 0)])


def spread_over(x, axes, dim):
    n = x.shape[dim]
    index = lax.axis_index(axes)
    total = lax.dynamic_index_in_dim(x, index, dim, keepdims=False)
    for shift in range(1, n):
        send = lax.dynamic_index_in_dim(x, (index + shift) % n, dim, keepdims=False)
        total = total + lax.ppermute(send, axes, [(i, (i + shift) % n) for i in range(n)])
    return total


def local(left_blocks, left_pattern, right_blocks, right_pattern):
    left = apply_pattern(left_blocks, left_pattern)
    right = apply_pattern(right_blocks, right_pattern).T
    left_rows = left.shape[0]
    cycle_size = lax.axis_size("row")
    position = lax.axis_index("row")
    zhi, ys, cores, layers = (lax.axis_size(a) for a in COL_PARTS + ("layer",))
    halves = ys // 2
    block = right.shape[0] // (halves * cores * layers)
    gathered = jnp.zeros((cycle_size, halves, block, left_rows), jnp.float32)
    arrived = right
    reduced = None
    for step in range(cycle_size):
        current = arrived
        if step > 0:
            if step + 1 < cycle_size:
                current, reduced = lax.optimization_barrier((current, reduced))
            else:
                left, reduced = lax.optimization_barrier((left, reduced))
            gathered = lax.dynamic_update_slice_in_dim(gathered, reduced[None], (position - step + 1) % cycle_size, 0)
        if step + 1 < cycle_size:
            arrived = from_behind(current, "row", 1)
        piece = lax.dot_general(current, left, (((1,), (1,)), ((), ())), preferred_element_type=jnp.float32)
        piece = piece.reshape(halves, cores, layers, block, left_rows)
        piece = pair_over(piece, "core", 1)
        reduced = spread_over(piece, "layer", 1)
    gathered = lax.dynamic_update_slice_in_dim(gathered, reduced[None], (position + 1) % cycle_size, 0)
    ordered = gathered.reshape(zhi, ys, block, left_rows)
    ordered = spread_over(ordered, "y", 1)
    ordered = pair_over(ordered, "zhi", 0)
    return ordered.T.astype(jnp.bfloat16)


def solution(mesh):
    cols = mesh.shape["col"]
    fine = Mesh(
        mesh.devices.reshape(mesh.shape["row"], 2, cols // 4, 2, mesh.shape["layer"]),
        ("row",) + COL_PARTS + ("layer",),
    )
    inner = ("layer",) + COL_PARTS
    placed = (
        P("row", inner),
        P("row", inner),
        P(inner, "row"),
        P(inner, "row"),
    )
    return jax.shard_map(
        local, mesh=fine, in_specs=placed, out_specs=P("row", COL_PARTS + ("layer",)), check_vma=False
    )
```

```python
import jax
import jax.numpy as jnp
from jax import lax
from jax.sharding import Mesh
from jax.sharding import PartitionSpec as P

COL_PARTS = ("zhi", "y", "core")


def from_behind(x, axis, by):
    size = lax.axis_size(axis)
    return lax.ppermute(x, axis, [(i, (i + by) % size) for i in range(size)])


def apply_pattern(values, pattern):
    rows, cols = values.shape
    block = rows // pattern.shape[0]
    widened = jnp.repeat(pattern.astype(jnp.bfloat16), cols // pattern.shape[1], axis=1)
    masked = values.reshape(pattern.shape[0], block, cols) * widened[:, None, :]
    return masked.reshape(rows, cols)


def pair_over(x, axis, dim):
    index = lax.axis_index(axis)
    keep = lax.dynamic_index_in_dim(x, index, dim, keepdims=False)
    send = lax.dynamic_index_in_dim(x, 1 - index, dim, keepdims=False)
    return keep + lax.ppermute(send, axis, [(0, 1), (1, 0)])


def spread_over(x, axes, dim):
    n = x.shape[dim]
    index = lax.axis_index(axes)
    total = lax.dynamic_index_in_dim(x, index, dim, keepdims=False)
    for shift in range(1, n):
        send = lax.dynamic_index_in_dim(x, (index + shift) % n, dim, keepdims=False)
        total = total + lax.ppermute(send, axes, [(i, (i + shift) % n) for i in range(n)])
    return total


def local(left_blocks, left_pattern, right_blocks, right_pattern):
    left = apply_pattern(left_blocks, left_pattern)
    right = apply_pattern(right_blocks, right_pattern).T
    left_rows = left.shape[0]
    cycle_size = lax.axis_size("row")
    position = lax.axis_index("row")
    zhi, ys, cores, layers = (lax.axis_size(a) for a in COL_PARTS + ("layer",))
    halves = ys // 2
    block = right.shape[0] // (halves * cores * layers)
    gathered = jnp.zeros((cycle_size, halves, block, left_rows), jnp.float32)
    arrived = right
    reduced = None
    for step in range(cycle_size):
        current = arrived
        if step > 0:
            if step + 1 < cycle_size:
                current, reduced = lax.optimization_barrier((current, reduced))
            else:
                left, reduced = lax.optimization_barrier((left, reduced))
            gathered = lax.dynamic_update_slice_in_dim(gathered, reduced[None], (position - step + 1) % cycle_size, 0)
        if step + 1 < cycle_size:
            arrived = from_behind(current, "row", 1)
        by_core = current.reshape(halves, cores, layers * block, current.shape[1])
        core = lax.axis_index("core")
        product = lambda rows: lax.dot_general(rows, left, (((2,), (1,)), ((), ())), preferred_element_type=jnp.float32)
        sent = lax.ppermute(product(lax.dynamic_index_in_dim(by_core, 1 - core, 1, keepdims=False)), "core", [(0, 1), (1, 0)])
        piece = product(lax.dynamic_index_in_dim(by_core, core, 1, keepdims=False)) + sent
        reduced = spread_over(piece.reshape(halves, layers, block, left_rows), "layer", 1)
    gathered = lax.dynamic_update_slice_in_dim(gathered, reduced[None], (position + 1) % cycle_size, 0)
    ordered = gathered.reshape(zhi, ys, block, left_rows)
    ordered = spread_over(ordered, "y", 1)
    ordered = pair_over(ordered, "zhi", 0)
    return ordered.T.astype(jnp.bfloat16)


def solution(mesh):
    cols = mesh.shape["col"]
    fine = Mesh(
        mesh.devices.reshape(mesh.shape["row"], 2, cols // 4, 2, mesh.shape["layer"]),
        ("row",) + COL_PARTS + ("layer",),
    )
    inner = ("layer",) + COL_PARTS
    placed = (
        P("row", inner),
        P("row", inner),
        P(inner, "row"),
        P(inner, "row"),
    )
    return jax.shard_map(
        local, mesh=fine, in_specs=placed, out_specs=P("row", COL_PARTS + ("layer",)), check_vma=False
    )
```

```python
import jax
import jax.numpy as jnp
from jax import lax
from jax.sharding import Mesh
from jax.sharding import PartitionSpec as P

COL_PARTS = ("zhi", "y", "core")


def from_behind(x, axis, by):
    size = lax.axis_size(axis)
    return lax.ppermute(x, axis, [(i, (i + by) % size) for i in range(size)])


def apply_pattern(values, pattern):
    rows, cols = values.shape
    block = rows // pattern.shape[0]
    widened = jnp.repeat(pattern.astype(jnp.bfloat16), cols // pattern.shape[1], axis=1)
    masked = values.reshape(pattern.shape[0], block, cols) * widened[:, None, :]
    return masked.reshape(rows, cols)


def pair_over(x, axis, dim):
    index = lax.axis_index(axis)
    keep = lax.dynamic_index_in_dim(x, index, dim, keepdims=False)
    send = lax.dynamic_index_in_dim(x, 1 - index, dim, keepdims=False)
    return keep + lax.ppermute(send, axis, [(0, 1), (1, 0)])


def spread_over(x, axes, dim):
    n = x.shape[dim]
    index = lax.axis_index(axes)
    total = lax.dynamic_index_in_dim(x, index, dim, keepdims=False)
    for shift in range(1, n):
        send = lax.dynamic_index_in_dim(x, (index + shift) % n, dim, keepdims=False)
        total = total + lax.ppermute(send, axes, [(i, (i + shift) % n) for i in range(n)])
    return total


def local(left_blocks, left_pattern, right_blocks, right_pattern):
    left = apply_pattern(left_blocks, left_pattern)
    right = apply_pattern(right_blocks, right_pattern).T
    left_rows = left.shape[0]
    cycle_size = lax.axis_size("row")
    position = lax.axis_index("row")
    zhi, ys, cores, layers = (lax.axis_size(a) for a in COL_PARTS + ("layer",))
    halves = ys // 2
    block = right.shape[0] // (halves * cores * layers)
    gathered = jnp.zeros((ys, zhi, block, left_rows), jnp.float32)
    store = lambda into, part, owner: lax.dynamic_update_slice(into, part[:, None], (owner % 2 * halves, owner // 2, 0, 0))
    arrived = right
    reduced = None
    for step in range(cycle_size):
        current = arrived
        if step > 0:
            if step + 1 < cycle_size:
                current, reduced = lax.optimization_barrier((current, reduced))
            else:
                left, reduced = lax.optimization_barrier((left, reduced))
            gathered = store(gathered, reduced, (position - step + 1) % cycle_size)
        if step + 1 < cycle_size:
            arrived = from_behind(current, "row", 1)
        piece = lax.dot_general(current, left, (((1,), (1,)), ((), ())), preferred_element_type=jnp.float32)
        piece = piece.reshape(halves, cores, layers, block, left_rows)
        piece = pair_over(piece, "core", 1)
        reduced = spread_over(piece, "layer", 1)
    gathered = store(gathered, reduced, (position + 1) % cycle_size)
    ordered = spread_over(gathered, "y", 0)
    ordered = pair_over(ordered, "zhi", 0)
    return ordered.T.astype(jnp.bfloat16)


def solution(mesh):
    cols = mesh.shape["col"]
    fine = Mesh(
        mesh.devices.reshape(mesh.shape["row"], 2, cols // 4, 2, mesh.shape["layer"]),
        ("row",) + COL_PARTS + ("layer",),
    )
    inner = ("layer",) + COL_PARTS
    placed = (
        P("row", inner),
        P("row", inner),
        P(inner, "row"),
        P(inner, "row"),
    )
    return jax.shard_map(
        local, mesh=fine, in_specs=placed, out_specs=P("row", COL_PARTS + ("layer",)), check_vma=False
    )
```

```python
import jax
import jax.numpy as jnp
from jax import lax
from jax.sharding import Mesh
from jax.sharding import PartitionSpec as P

COL_PARTS = ("zhi", "y", "core")


def from_behind(x, axis, by):
    size = lax.axis_size(axis)
    return lax.ppermute(x, axis, [(i, (i + by) % size) for i in range(size)])


def apply_pattern(values, pattern):
    rows, cols = values.shape
    block = rows // pattern.shape[0]
    widened = jnp.repeat(pattern.astype(jnp.bfloat16), cols // pattern.shape[1], axis=1)
    masked = values.reshape(pattern.shape[0], block, cols) * widened[:, None, :]
    return masked.reshape(rows, cols)


def pair_over(x, axis, dim):
    index = lax.axis_index(axis)
    keep = lax.dynamic_index_in_dim(x, index, dim, keepdims=False)
    send = lax.dynamic_index_in_dim(x, 1 - index, dim, keepdims=False)
    return keep + lax.ppermute(send, axis, [(0, 1), (1, 0)])


def spread_over(x, axes, dim):
    n = x.shape[dim]
    index = lax.axis_index(axes)
    total = lax.dynamic_index_in_dim(x, index, dim, keepdims=False)
    for shift in range(1, n):
        send = lax.dynamic_index_in_dim(x, (index + shift) % n, dim, keepdims=False)
        total = total + lax.ppermute(send, axes, [(i, (i + shift) % n) for i in range(n)])
    return total


def local(left_blocks, left_pattern, right_blocks, right_pattern):
    left = apply_pattern(left_blocks, left_pattern)
    right = apply_pattern(right_blocks.T, right_pattern.T)
    left_rows = left.shape[0]
    cycle_size = lax.axis_size("row")
    position = lax.axis_index("row")
    zhi, ys, cores, layers = (lax.axis_size(a) for a in COL_PARTS + ("layer",))
    halves = ys // 2
    block = right.shape[0] // (halves * cores * layers)
    gathered = jnp.zeros((cycle_size, halves, block, left_rows), jnp.float32)
    arrived = right
    reduced = None
    for step in range(cycle_size):
        current = arrived
        if step > 0:
            if step + 1 < cycle_size:
                current, reduced = lax.optimization_barrier((current, reduced))
            else:
                left, reduced = lax.optimization_barrier((left, reduced))
            gathered = lax.dynamic_update_slice_in_dim(gathered, reduced[None], (position - step + 1) % cycle_size, 0)
        if step + 1 < cycle_size:
            arrived = from_behind(current, "row", 1)
        piece = lax.dot_general(current, left, (((1,), (1,)), ((), ())), preferred_element_type=jnp.float32)
        piece = piece.reshape(halves, cores, layers, block, left_rows)
        piece = pair_over(piece, "core", 1)
        reduced = spread_over(piece, "layer", 1)
    gathered = lax.dynamic_update_slice_in_dim(gathered, reduced[None], (position + 1) % cycle_size, 0)
    ordered = gathered.reshape(zhi, ys, block, left_rows)
    ordered = spread_over(ordered, "y", 1)
    ordered = pair_over(ordered, "zhi", 0)
    return ordered.T.astype(jnp.bfloat16)


def solution(mesh):
    cols = mesh.shape["col"]
    fine = Mesh(
        mesh.devices.reshape(mesh.shape["row"], 2, cols // 4, 2, mesh.shape["layer"]),
        ("row",) + COL_PARTS + ("layer",),
    )
    inner = ("layer",) + COL_PARTS
    placed = (
        P("row", inner),
        P("row", inner),
        P(inner, "row"),
        P(inner, "row"),
    )
    return jax.shard_map(
        local, mesh=fine, in_specs=placed, out_specs=P("row", COL_PARTS + ("layer",)), check_vma=False
    )
```

```python
import jax
import jax.numpy as jnp
from jax import lax
from jax.sharding import Mesh
from jax.sharding import PartitionSpec as P

COL_PARTS = ("zhi", "y", "core")


def from_behind(x, axis, by):
    size = lax.axis_size(axis)
    return lax.ppermute(x, axis, [(i, (i + by) % size) for i in range(size)])


def apply_pattern(values, pattern):
    rows, cols = values.shape
    block = rows // pattern.shape[0]
    widened = jnp.repeat(pattern.astype(jnp.bfloat16), cols // pattern.shape[1], axis=1)
    masked = values.reshape(pattern.shape[0], block, cols) * widened[:, None, :]
    return masked.reshape(rows, cols)


def pair_over(x, axis, dim):
    index = lax.axis_index(axis)
    keep = lax.dynamic_index_in_dim(x, index, dim, keepdims=False)
    send = lax.dynamic_index_in_dim(x, 1 - index, dim, keepdims=False)
    return keep + lax.ppermute(send, axis, [(0, 1), (1, 0)])


def spread_over(x, axes, dim):
    n = x.shape[dim]
    index = lax.axis_index(axes)
    total = lax.dynamic_index_in_dim(x, index, dim, keepdims=False)
    for shift in range(1, n):
        send = lax.dynamic_index_in_dim(x, (index + shift) % n, dim, keepdims=False)
        total = total + lax.ppermute(send, axes, [(i, (i + shift) % n) for i in range(n)])
    return total


def local(left_blocks, left_pattern, right_blocks, right_pattern):
    left = apply_pattern(left_blocks, left_pattern)
    right = apply_pattern(right_blocks.T, right_pattern.T)
    left_rows = left.shape[0]
    cycle_size = lax.axis_size("row")
    position = lax.axis_index("row")
    zhi, ys, cores, layers = (lax.axis_size(a) for a in COL_PARTS + ("layer",))
    halves = ys // 2
    block = right.shape[0] // (halves * cores * layers)
    right = right.reshape(halves, cores, layers, block, -1).transpose(1, 2, 0, 3, 4).reshape(right.shape)
    gathered = jnp.zeros((cycle_size, halves, block, left_rows), jnp.float32)
    arrived = right
    reduced = None
    for step in range(cycle_size):
        current = arrived
        if step > 0:
            if step + 1 < cycle_size:
                current, reduced = lax.optimization_barrier((current, reduced))
            else:
                left, reduced = lax.optimization_barrier((left, reduced))
            gathered = lax.dynamic_update_slice_in_dim(gathered, reduced[None], (position - step + 1) % cycle_size, 0)
        if step + 1 < cycle_size:
            arrived = from_behind(current, "row", 1)
        piece = lax.dot_general(current, left, (((1,), (1,)), ((), ())), preferred_element_type=jnp.float32)
        piece = piece.reshape(cores, layers, halves, block, left_rows)
        piece = pair_over(piece, "core", 0)
        reduced = spread_over(piece, "layer", 0)
    gathered = lax.dynamic_update_slice_in_dim(gathered, reduced[None], (position + 1) % cycle_size, 0)
    ordered = gathered.reshape(zhi, ys, block, left_rows)
    ordered = spread_over(ordered, "y", 1)
    ordered = pair_over(ordered, "zhi", 0)
    return ordered.T.astype(jnp.bfloat16)


def solution(mesh):
    cols = mesh.shape["col"]
    fine = Mesh(
        mesh.devices.reshape(mesh.shape["row"], 2, cols // 4, 2, mesh.shape["layer"]),
        ("row",) + COL_PARTS + ("layer",),
    )
    inner = ("layer",) + COL_PARTS
    placed = (
        P("row", inner),
        P("row", inner),
        P(inner, "row"),
        P(inner, "row"),
    )
    return jax.shard_map(
        local, mesh=fine, in_specs=placed, out_specs=P("row", COL_PARTS + ("layer",)), check_vma=False
    )
```

```python
import jax
import jax.numpy as jnp
from jax import lax
from jax.sharding import Mesh
from jax.sharding import PartitionSpec as P

COL_PARTS = ("zhi", "y", "core")


def from_behind(x, axis, by):
    size = lax.axis_size(axis)
    return lax.ppermute(x, axis, [(i, (i + by) % size) for i in range(size)])


def apply_pattern(values, pattern):
    rows, cols = values.shape
    block = rows // pattern.shape[0]
    widened = jnp.repeat(pattern.astype(jnp.bfloat16), cols // pattern.shape[1], axis=1)
    masked = values.reshape(pattern.shape[0], block, cols) * widened[:, None, :]
    return masked.reshape(rows, cols)


def pair_over(x, axis, dim):
    index = lax.axis_index(axis)
    keep = lax.dynamic_index_in_dim(x, index, dim, keepdims=False)
    send = lax.dynamic_index_in_dim(x, 1 - index, dim, keepdims=False)
    return keep + lax.ppermute(send, axis, [(0, 1), (1, 0)])


def spread_over(x, axes, dim):
    n = x.shape[dim]
    index = lax.axis_index(axes)
    total = lax.dynamic_index_in_dim(x, index, dim, keepdims=False)
    for shift in range(1, n):
        send = lax.dynamic_index_in_dim(x, (index + shift) % n, dim, keepdims=False)
        total = total + lax.ppermute(send, axes, [(i, (i + shift) % n) for i in range(n)])
    return total


def local(left_blocks, left_pattern, right_blocks, right_pattern):
    left = apply_pattern(left_blocks, left_pattern)
    right = apply_pattern(right_blocks.T, right_pattern.T)
    left_rows = left.shape[0]
    cycle_size = lax.axis_size("row")
    position = lax.axis_index("row")
    zhi, ys, cores, layers = (lax.axis_size(a) for a in COL_PARTS + ("layer",))
    halves = ys // 2
    block = right.shape[0] // (halves * cores * layers)
    gathered = jnp.zeros((ys, zhi, block, left_rows), jnp.float32)
    store = lambda into, part, owner: lax.dynamic_update_slice(into, part[:, None], (owner % 2 * halves, owner // 2, 0, 0))
    arrived = right
    reduced = None
    for step in range(cycle_size):
        current = arrived
        if step > 0:
            if step + 1 < cycle_size:
                current, reduced = lax.optimization_barrier((current, reduced))
            else:
                left, reduced = lax.optimization_barrier((left, reduced))
            gathered = store(gathered, reduced, (position - step + 1) % cycle_size)
        if step + 1 < cycle_size:
            arrived = from_behind(current, "row", 1)
        piece = lax.dot_general(current, left, (((1,), (1,)), ((), ())), preferred_element_type=jnp.float32)
        piece = piece.reshape(halves, cores, layers, block, left_rows)
        piece = pair_over(piece, "core", 1)
        reduced = spread_over(piece, "layer", 1)
    gathered = store(gathered, reduced, (position + 1) % cycle_size)
    ordered = spread_over(gathered, "y", 0)
    ordered = pair_over(ordered, "zhi", 0)
    return ordered.T.astype(jnp.bfloat16)


def solution(mesh):
    cols = mesh.shape["col"]
    fine = Mesh(
        mesh.devices.reshape(mesh.shape["row"], 2, cols // 4, 2, mesh.shape["layer"]),
        ("row",) + COL_PARTS + ("layer",),
    )
    inner = ("layer",) + COL_PARTS
    placed = (
        P("row", inner),
        P("row", inner),
        P(inner, "row"),
        P(inner, "row"),
    )
    return jax.shard_map(
        local, mesh=fine, in_specs=placed, out_specs=P("row", COL_PARTS + ("layer",)), check_vma=False
    )
```
